512 devices in a mesh: fsdp: 128 (over z, y, core), tp: 4 (over x).
Axes of the slice: x: 4, y: 8, z: 8, core: 2. Of those that a mesh axis runs over, the one named last changes fastest.
Arguments:
- q_grad: bfloat16 [128, 1280, 768], P('fsdp', None, 'tp'), may hold values from -24 to 24, as said below
- o_grad: bfloat16 [128, 768, 1280], P('fsdp', 'tp'), may hold values from -24 to 24, as said below
- norm_grad: float32 [128, 4, 1344], P('fsdp', 'tp'), may hold values from -6 to 6, as said below
- emb_grad: bfloat16 [8192, 1280], P('fsdp', 'tp'), may hold values from -6 to 6, as said below
- flat_master: float32 [4, 491520], P('tp', 'fsdp'), may hold values from -0.15625 to 0.15625
- flat_first: float32 [4, 491520], P('tp', 'fsdp'), may hold values from -0.75 to 0.75
- flat_second: float32 [4, 491520], P('tp', 'fsdp'), may hold values from 0.001 to 0.1
- emb_master: float32 [8192, 1280], P(('fsdp', 'tp')), may hold values from -0.3125 to 0.3125
- emb_first: float32 [8192, 1280], P(('fsdp', 'tp')), may hold values from -0.75 to 0.75
- emb_second: float32 [8192, 1280], P(('fsdp', 'tp')), may hold values from 0.001 to 0.1
- norm_master: float32 [1344], replicated, may hold values from 0.5 to 1.5
- norm_first: float32 [1344], replicated, may hold values from -0.75 to 0.75
- norm_second: float32 [1344], replicated, may hold values from 0.001 to 0.1
- step_count: int32 [1], replicated, may hold values from 1 to 64
Outputs:
- new_flat_master: float32 [4, 491520], P('tp', 'fsdp')
- new_flat_first: float32 [4, 491520], P('tp', 'fsdp')
- new_flat_second: float32 [4, 491520], P('tp', 'fsdp')
- new_emb_master: float32 [8192, 1280], P(('fsdp', 'tp'))
- new_emb_first: float32 [8192, 1280], P(('fsdp', 'tp'))
- new_emb_second: float32 [8192, 1280], P(('fsdp', 'tp'))
- new_norm_master: float32 [1344], replicated
- new_norm_first: float32 [1344], replicated
- new_norm_second: float32 [1344], replicated
- q_weight: bfloat16 [1280, 768], P(None, 'tp')
- o_weight: bfloat16 [768, 1280], P('tp')
- q_average: bfloat16 [1280, 768], P('fsdp')
- o_average: bfloat16 [768, 1280], P(None, 'fsdp')
- emb_weight: bfloat16 [8192, 1280], P('fsdp', 'tp')
The draws below stay inside these ranges and needn't reach their ends.
Inputs may be any that keep to these rules, and one draw needn't show every extreme that they name: `q_grad`: each data replica's gradient of the query projection. `o_grad`: each data replica's gradient of the output projection. `norm_grad`: each device's gradient of the gains. `emb_grad`: the embedding slice's summed gradient.
All inputs are finite; a program needn't handle non-finite values.
Results may differ from the reference program's by a relative error of at most 0.0004.
Values may be sent and summed in bfloat16 or wider, within the bound.
No kernel may reach another device: no remote copies, remote signals or barrier semaphores. Data moves between devices by JAX's collectives and lax.ppermute only.
A program may use at most 64 MiB of HBM per device.

```python
import math
import jax
import jax.numpy as jnp
from jax import lax

D = 1280
QW = 768
EMB = 8192
FLAT = 491520
NORMS = 1344
COUNT = 12453184
N_FSDP = 128
N_TP = 4


def rising(position):
    ratio = 6.0
    return jnp.exp(0.5 * math.log(ratio) * (position - 1.0)).astype(jnp.float32)


def drawn_values(key, shape):
    return jnp.clip(jax.random.normal(key, shape, jnp.float32), -6.0, 6.0)


def spiked_values(key, shape):
    common_weight = 0.35
    own_weight = 0.95
    own_part = jax.random.normal(jax.random.fold_in(key, 1), shape, jnp.float32)
    shared_part = jax.random.normal(jax.random.fold_in(key, 3), shape[1:], jnp.float32)
    values = jnp.clip(common_weight * shared_part[None, :, :] + own_weight * own_part, -6.0, 6.0)
    pairing = jax.random.permutation(jax.random.fold_in(key, 2), N_FSDP)
    rows = shape[1]
    row_block = jnp.arange(rows, dtype=jnp.int32) * N_FSDP // rows
    hit = pairing[:, None] == row_block[None, :]
    factor = jnp.where(hit, 4.0, 1.0).astype(jnp.float32)
    return values * factor[:, :, None]


def draw_q_grad(key, part):
    values = spiked_values(jax.random.fold_in(key, 11), (N_FSDP, D, QW))
    position = 0.5 * jnp.arange(D, dtype=jnp.float32) / D
    return (values * rising(position)[None, :, None]).astype(jnp.bfloat16)


def draw_o_grad(key, part):
    values = spiked_values(jax.random.fold_in(key, 12), (N_FSDP, QW, D))
    columns = QW // N_TP
    inner = (jnp.arange(QW, dtype=jnp.int32) % columns).astype(jnp.float32)
    position = 0.5 + 0.5 * inner / columns
    return (values * rising(position)[None, :, None]).astype(jnp.bfloat16)


def draw_norm_grad(key, part):
    return drawn_values(jax.random.fold_in(key, 13), (N_FSDP, N_TP, NORMS))


def draw_emb_grad(key, part):
    values = drawn_values(jax.random.fold_in(key, 14), (EMB, D))
    position = jnp.arange(EMB, dtype=jnp.float32) / EMB
    return (values * rising(position)[:, None]).astype(jnp.bfloat16)


def level_of(rng, dims, pieces, smallest, high):
    loudness, own = 1.0, jax.random.fold_in(rng, 6)
    for dim, parts in pieces:
        heights = jnp.exp(jax.random.uniform(jax.random.fold_in(own, dim), (parts,), jnp.float32, smallest / len(pieces), high / len(pieces)))
        loudness = loudness * jnp.repeat(heights, dims[dim] // parts).reshape([-1 if axis == dim else 1 for axis in range(len(dims))])
    return loudness


def gaussian(key, dims, width, reach, shards=(), kind=jnp.bfloat16):
    result = width * jax.random.normal(key, dims, jnp.float32)
    if shards:
        result = result * level_of(key, dims, shards, -0.22, 0.18)
    return jnp.clip(result, -reach, reach).astype(kind)


def setup_inputs(seed: int = 0) -> dict:
    key_list = jax.random.split(jax.random.key(seed), 15)
    return {
        "q_grad": draw_q_grad(jax.random.fold_in(key_list[14], 71), 0),
        "o_grad": draw_o_grad(jax.random.fold_in(key_list[14], 71), 0),
        "norm_grad": draw_norm_grad(jax.random.fold_in(key_list[14], 71), 0),
        "emb_grad": draw_emb_grad(jax.random.fold_in(key_list[14], 71), 0),
        "flat_master": gaussian(key_list[4], (N_TP, FLAT), D ** -0.5, 0.15625, ((0, 4), (1, 128)), jnp.float32),
        "flat_first": gaussian(key_list[5], (N_TP, FLAT), 0.05, 0.75, ((0, 4), (1, 128)), jnp.float32),
        "flat_second": jnp.clip(jnp.exp(math.log(0.1) - 4.6051702 * jax.random.uniform(key_list[6], (N_TP, FLAT), jnp.float32) ** level_of(key_list[6], (N_TP, FLAT), ((0, 4), (1, 128)), -0.2, 0.2)), 0.001, 0.1),
        "emb_master": gaussian(key_list[7], (EMB, D), 0.02, 0.3125, ((0, 512),), jnp.float32),
        "emb_first": gaussian(key_list[8], (EMB, D), 0.05, 0.75, ((0, 512),), jnp.float32),
        "emb_second": jnp.clip(jnp.exp(math.log(0.1) - 4.6051702 * jax.random.uniform(key_list[9], (EMB, D), jnp.float32) ** level_of(key_list[9], (EMB, D), ((0, 512),), -0.2, 0.2)), 0.001, 0.1),
        "norm_master": jnp.clip(1.0 + 0.1 * jax.random.normal(key_list[10], (NORMS,), jnp.float32), 0.5, 1.5),
        "norm_first": gaussian(key_list[11], (NORMS,), 0.05, 0.75, (), jnp.float32),
        "norm_second": jnp.clip(jnp.exp(jax.random.uniform(key_list[12], (NORMS,), jnp.float32, math.log(0.001), math.log(0.1))), 0.001, 0.1),
        "step_count": jax.random.randint(key_list[13], (1,), 1, 65).astype(jnp.int32),
    }


BETA_ONE = 0.9
BETA_TWO = 0.95
EPSILON = 1e-08
LEARN_RATE = 0.0053

def adam_update(weights_in, first_in, second_in, gradient, first_fix, second_fix, decay_rate):
    first_out = BETA_ONE * first_in + (1.0 - BETA_ONE) * gradient
    second_out = BETA_TWO * second_in + (1.0 - BETA_TWO) * gradient * gradient
    update = first_out / first_fix / (jnp.sqrt(second_out / second_fix) + EPSILON)
    weights_out = weights_in - LEARN_RATE * (update + decay_rate * weights_in)
    return (weights_out, first_out, second_out)

def reference(q_grad, o_grad, norm_grad, emb_grad, flat_master, flat_first, flat_second, emb_master, emb_first, emb_second, norm_master, norm_first, norm_second, step_count):
    q_sum = lax.optimization_barrier(jnp.sum(q_grad.astype(jnp.float32), axis=0))
    o_sum = lax.optimization_barrier(jnp.sum(o_grad.astype(jnp.float32), axis=0))
    columns = QW // N_TP
    q_parts = q_sum.reshape(D, N_TP, columns).transpose(1, 0, 2).reshape(N_TP, D * columns)
    o_parts = o_sum.reshape(N_TP, columns * D)
    grad_flat = jnp.concatenate([q_parts, o_parts], axis=1)
    gain_sum = lax.optimization_barrier(jnp.sum(norm_grad, axis=(0, 1)))
    emb_float = emb_grad.astype(jnp.float32)
    squared = jnp.sum(grad_flat * grad_flat) + jnp.sum(emb_float * emb_float) + jnp.sum(gain_sum * gain_sum)
    grad_norm = jnp.sqrt(squared)
    clip_limit = 0.5 * math.sqrt(COUNT)
    clip_factor = jnp.minimum(jnp.float32(1.0), clip_limit / (grad_norm + 1e-06))
    step_value = step_count[0].astype(jnp.float32)
    first_fix = 1.0 - jnp.power(jnp.float32(BETA_ONE), step_value)
    second_fix = 1.0 - jnp.power(jnp.float32(BETA_TWO), step_value)
    flat_new, flat_one, flat_two = adam_update(flat_master, flat_first, flat_second, clip_factor * grad_flat, first_fix, second_fix, 0.1)
    emb_new, emb_one, emb_two = adam_update(emb_master, emb_first, emb_second, clip_factor * emb_float, first_fix, second_fix, 0.1)
    norm_new, norm_one, norm_two = adam_update(norm_master, norm_first, norm_second, clip_factor * gain_sum, first_fix, second_fix, 0.0)
    flat_bf = flat_new.astype(jnp.bfloat16)
    q_weight = flat_bf[:, :D * columns].reshape(N_TP, D, columns).transpose(1, 0, 2).reshape(D, QW)
    o_weight = flat_bf[:, D * columns:].reshape(QW, D)
    emb_weight = emb_new.astype(jnp.bfloat16)
    return (flat_new, flat_one, flat_two, emb_new, emb_one, emb_two, norm_new, norm_one, norm_two, q_weight, o_weight, q_weight, o_weight, emb_weight)
```

```python
import math

import jax
import jax.numpy as jnp
from jax import lax
from jax.sharding import Mesh
from jax.sharding import PartitionSpec as P

BETA_ONE = 0.9
BETA_TWO = 0.95
EPSILON = 1e-08
LEARN_RATE = 0.0053

FSDP = ("z", "y", "c")
CORES = 2
Y_SIZE = 8


def adam_update(weights_in, first_in, second_in, gradient, first_fix, second_fix, decay_rate):
    first_out = BETA_ONE * first_in + (1.0 - BETA_ONE) * gradient
    second_out = BETA_TWO * second_in + (1.0 - BETA_TWO) * gradient * gradient
    update = first_out / first_fix / (jnp.sqrt(second_out / second_fix) + EPSILON)
    weights_out = weights_in - LEARN_RATE * (update + decay_rate * weights_in)
    return (weights_out, first_out, second_out)


def fsdp_index():
    return (
        lax.axis_index("z") * (Y_SIZE * CORES)
        + lax.axis_index("y") * CORES
        + lax.axis_index("c")
    )


def body(
    q_grad,
    o_grad,
    norm_grad,
    emb_grad,
    flat_master,
    flat_first,
    flat_second,
    emb_master,
    emb_first,
    emb_second,
    norm_master,
    norm_first,
    norm_second,
    step_count,
):
    fsdp_count = lax.axis_size(FSDP)
    tp_count = lax.axis_size("tp")
    width = q_grad.shape[1]
    q_columns = q_grad.shape[2]
    entry_count = (
        2 * width * q_columns * tp_count
        + emb_grad.shape[0] * fsdp_count * width
        + norm_master.shape[0]
    )
    clip_limit = 0.5 * math.sqrt(entry_count)
    local_flat = jnp.concatenate([q_grad[0].reshape(-1), o_grad[0].reshape(-1)])
    piece_len = local_flat.shape[0] // fsdp_count
    pieces = lax.all_to_all(
        local_flat.reshape(fsdp_count, piece_len), FSDP, 0, 0, tiled=True
    )
    grad_piece = jnp.sum(pieces.astype(jnp.float32), axis=0)
    emb_piece = lax.all_to_all(emb_grad, "tp", split_axis=0, concat_axis=1, tiled=True).astype(
        jnp.float32
    )
    local_squares = jnp.sum(grad_piece * grad_piece) + jnp.sum(emb_piece * emb_piece)
    gains_local = norm_grad[0, 0]
    packed = jnp.concatenate([local_squares[None], gains_local])
    for axis in ("c", "tp", "y", "z"):
        packed = lax.psum(packed, axis)
    global_squares = packed[0]
    gain_sum = packed[1:]
    grad_norm = jnp.sqrt(global_squares + jnp.sum(gain_sum * gain_sum))
    clip_factor = jnp.minimum(jnp.float32(1.0), clip_limit / (grad_norm + 1e-06))
    step_value = step_count[0].astype(jnp.float32)
    first_fix = 1.0 - jnp.power(jnp.float32(BETA_ONE), step_value)
    second_fix = 1.0 - jnp.power(jnp.float32(BETA_TWO), step_value)
    flat_new, flat_one, flat_two = adam_update(
        flat_master[0],
        flat_first[0],
        flat_second[0],
        clip_factor * grad_piece,
        first_fix,
        second_fix,
        0.1,
    )
    emb_new, emb_one, emb_two = adam_update(
        emb_master, emb_first, emb_second, clip_factor * emb_piece, first_fix, second_fix, 0.1
    )
    norm_new, norm_one, norm_two = adam_update(
        norm_master, norm_first, norm_second, clip_factor * gain_sum, first_fix, second_fix, 0.0
    )
    gathered = lax.all_gather(flat_new.astype(jnp.bfloat16), "c", axis=0, tiled=False)
    gathered = lax.all_gather(gathered, ("z", "y"), axis=0, tiled=False).reshape(-1)
    q_weight = gathered[: width * q_columns].reshape(width, q_columns)
    o_weight = gathered[width * q_columns :].reshape(q_columns, width)
    block_rows = width // fsdp_count
    block_start = fsdp_index() * block_rows
    q_block = lax.dynamic_slice_in_dim(q_weight, block_start, block_rows, 0)
    o_block = lax.dynamic_slice_in_dim(o_weight, block_start, block_rows, 1)
    emb_rows = emb_new.astype(jnp.bfloat16)
    payload = jnp.concatenate([q_block.reshape(-1), o_block.reshape(-1), emb_rows.reshape(-1)])
    shared = lax.all_gather(payload, "tp", axis=0, tiled=False)
    q_len = block_rows * q_columns
    q_average = (
        shared[:, :q_len]
        .reshape(tp_count, block_rows, q_columns)
        .transpose(1, 0, 2)
        .reshape(block_rows, tp_count * q_columns)
    )
    o_average = shared[:, q_len : 2 * q_len].reshape(tp_count * q_columns, block_rows)
    emb_all = shared[:, 2 * q_len :].reshape(tp_count * emb_new.shape[0], width)
    emb_cols = width // tp_count
    emb_weight = lax.dynamic_slice_in_dim(emb_all, lax.axis_index("tp") * emb_cols, emb_cols, 1)
    return (
        flat_new[None, :],
        flat_one[None, :],
        flat_two[None, :],
        emb_new,
        emb_one,
        emb_two,
        norm_new,
        norm_one,
        norm_two,
        q_weight,
        o_weight,
        q_average,
        o_average,
        emb_weight,
    )


def solution(mesh):
    fsdp_count = mesh.shape["fsdp"]
    tp_count = mesh.shape["tp"]
    split = Mesh(
        mesh.devices.reshape(fsdp_count // (Y_SIZE * CORES), Y_SIZE, CORES, tp_count),
        ("z", "y", "c", "tp"),
    )
    both = FSDP + ("tp",)
    return jax.shard_map(
        body,
        mesh=split,
        in_specs=(
            P(FSDP, None, "tp"),
            P(FSDP, "tp", None),
            P(FSDP, "tp", None),
            P(FSDP, "tp"),
            P("tp", FSDP),
            P("tp", FSDP),
            P("tp", FSDP),
            P(both, None),
            P(both, None),
            P(both, None),
            P(),
            P(),
            P(),
            P(),
        ),
        out_specs=(
            P("tp", FSDP),
            P("tp", FSDP),
            P("tp", FSDP),
            P(both, None),
            P(both, None),
            P(both, None),
            P(),
            P(),
            P(),
            P(None, "tp"),
            P("tp", None),
            P(FSDP, None),
            P(None, FSDP),
            P(FSDP, "tp"),
        ),
        check_vma=False,
    )
```

```python
import math

import jax
import jax.numpy as jnp
from jax import lax
from jax.sharding import Mesh
from jax.sharding import PartitionSpec as P

BETA_ONE = 0.9
BETA_TWO = 0.95
EPSILON = 1e-08
LEARN_RATE = 0.0053

FSDP = ("z", "y", "c")
CORES = 2
Y_SIZE = 8


def adam_update(weights_in, first_in, second_in, gradient, first_fix, second_fix, decay_rate):
    first_out = BETA_ONE * first_in + (1.0 - BETA_ONE) * gradient
    second_out = BETA_TWO * second_in + (1.0 - BETA_TWO) * gradient * gradient
    update = first_out / first_fix / (jnp.sqrt(second_out / second_fix) + EPSILON)
    weights_out = weights_in - LEARN_RATE * (update + decay_rate * weights_in)
    return (weights_out, first_out, second_out)


def fsdp_index():
    return (
        lax.axis_index("z") * (Y_SIZE * CORES)
        + lax.axis_index("y") * CORES
        + lax.axis_index("c")
    )


def body(
    q_grad,
    o_grad,
    norm_grad,
    emb_grad,
    flat_master,
    flat_first,
    flat_second,
    emb_master,
    emb_first,
    emb_second,
    norm_master,
    norm_first,
    norm_second,
    step_count,
):
    fsdp_count = lax.axis_size(FSDP)
    tp_count = lax.axis_size("tp")
    width = q_grad.shape[1]
    q_columns = q_grad.shape[2]
    entry_count = (
        2 * width * q_columns * tp_count
        + emb_grad.shape[0] * fsdp_count * width
        + norm_master.shape[0]
    )
    clip_limit = 0.5 * math.sqrt(entry_count)
    local_flat = jnp.concatenate([q_grad[0].reshape(-1), o_grad[0].reshape(-1)])
    piece_len = local_flat.shape[0] // fsdp_count
    pieces = lax.all_to_all(
        local_flat.reshape(fsdp_count, piece_len), FSDP, 0, 0, tiled=True
    )
    grad_piece = jnp.sum(pieces.astype(jnp.float32), axis=0)
    emb_piece = lax.all_to_all(emb_grad, "tp", split_axis=0, concat_axis=1, tiled=True).astype(
        jnp.float32
    )
    local_squares = jnp.sum(grad_piece * grad_piece) + jnp.sum(emb_piece * emb_piece)
    gains_local = norm_grad[0, 0]
    packed = jnp.concatenate([local_squares[None], gains_local])
    for axis in (("y", "c"), "z", "tp"):
        count = lax.axis_size(axis)
        copies = jnp.broadcast_to(packed[None], (count,) + packed.shape)
        packed = jnp.sum(lax.all_to_all(copies, axis, 0, 0, tiled=True), axis=0)
    global_squares = packed[0]
    gain_sum = packed[1:]
    grad_norm = jnp.sqrt(global_squares + jnp.sum(gain_sum * gain_sum))
    clip_factor = jnp.minimum(jnp.float32(1.0), clip_limit / (grad_norm + 1e-06))
    step_value = step_count[0].astype(jnp.float32)
    first_fix = 1.0 - jnp.power(jnp.float32(BETA_ONE), step_value)
    second_fix = 1.0 - jnp.power(jnp.float32(BETA_TWO), step_value)
    flat_new, flat_one, flat_two = adam_update(
        flat_master[0],
        flat_first[0],
        flat_second[0],
        clip_factor * grad_piece,
        first_fix,
        second_fix,
        0.1,
    )
    emb_new, emb_one, emb_two = adam_update(
        emb_master, emb_first, emb_second, clip_factor * emb_piece, first_fix, second_fix, 0.1
    )
    norm_new, norm_one, norm_two = adam_update(
        norm_master, norm_first, norm_second, clip_factor * gain_sum, first_fix, second_fix, 0.0
    )
    gathered = lax.all_gather(flat_new.astype(jnp.bfloat16), ("y", "c"), axis=0, tiled=False)
    gathered = lax.all_gather(gathered, "z", axis=0, tiled=False).reshape(-1)
    q_weight = gathered[: width * q_columns].reshape(width, q_columns)
    o_weight = gathered[width * q_columns :].reshape(q_columns, width)
    block_rows = width // fsdp_count
    block_start = fsdp_index() * block_rows
    q_block = lax.dynamic_slice_in_dim(q_weight, block_start, block_rows, 0)
    o_block = lax.dynamic_slice_in_dim(o_weight, block_start, block_rows, 1)
    emb_rows = emb_new.astype(jnp.bfloat16)
    payload = jnp.concatenate([q_block.reshape(-1), o_block.reshape(-1), emb_rows.reshape(-1)])
    shared = lax.all_gather(payload, "tp", axis=0, tiled=False)
    q_len = block_rows * q_columns
    q_average = (
        shared[:, :q_len]
        .reshape(tp_count, block_rows, q_columns)
        .transpose(1, 0, 2)
        .reshape(block_rows, tp_count * q_columns)
    )
    o_average = shared[:, q_len : 2 * q_len].reshape(tp_count * q_columns, block_rows)
    emb_all = shared[:, 2 * q_len :].reshape(tp_count * emb_new.shape[0], width)
    emb_cols = width // tp_count
    emb_weight = lax.dynamic_slice_in_dim(emb_all, lax.axis_index("tp") * emb_cols, emb_cols, 1)
    return (
        flat_new[None, :],
        flat_one[None, :],
        flat_two[None, :],
        emb_new,
        emb_one,
        emb_two,
        norm_new,
        norm_one,
        norm_two,
        q_weight,
        o_weight,
        q_average,
        o_average,
        emb_weight,
    )


def solution(mesh):
    fsdp_count = mesh.shape["fsdp"]
    tp_count = mesh.shape["tp"]
    split = Mesh(
        mesh.devices.reshape(fsdp_count // (Y_SIZE * CORES), Y_SIZE, CORES, tp_count),
        ("z", "y", "c", "tp"),
    )
    both = FSDP + ("tp",)
    return jax.shard_map(
        body,
        mesh=split,
        in_specs=(
            P(FSDP, None, "tp"),
            P(FSDP, "tp", None),
            P(FSDP, "tp", None),
            P(FSDP, "tp"),
            P("tp", FSDP),
            P("tp", FSDP),
            P("tp", FSDP),
            P(both, None),
            P(both, None),
            P(both, None),
            P(),
            P(),
            P(),
            P(),
        ),
        out_specs=(
            P("tp", FSDP),
            P("tp", FSDP),
            P("tp", FSDP),
            P(both, None),
            P(both, None),
            P(both, None),
            P(),
            P(),
            P(),
            P(None, "tp"),
            P("tp", None),
            P(FSDP, None),
            P(None, FSDP),
            P(FSDP, "tp"),
        ),
        check_vma=False,
    )
```

```python
import math

import jax
import jax.numpy as jnp
from jax import lax
from jax.sharding import Mesh
from jax.sharding import PartitionSpec as P

BETA_ONE = 0.9
BETA_TWO = 0.95
EPSILON = 1e-08
LEARN_RATE = 0.0053

FSDP = ("z", "y", "c")
CORES = 2
Y_SIZE = 8


def adam_update(weights_in, first_in, second_in, gradient, first_fix, second_fix, decay_rate):
    first_out = BETA_ONE * first_in + (1.0 - BETA_ONE) * gradient
    second_out = BETA_TWO * second_in + (1.0 - BETA_TWO) * gradient * gradient
    update = first_out / first_fix / (jnp.sqrt(second_out / second_fix) + EPSILON)
    weights_out = weights_in - LEARN_RATE * (update + decay_rate * weights_in)
    return (weights_out, first_out, second_out)


def fsdp_index():
    return (
        lax.axis_index("z") * (Y_SIZE * CORES)
        + lax.axis_index("y") * CORES
        + lax.axis_index("c")
    )


def body(
    q_grad,
    o_grad,
    norm_grad,
    emb_grad,
    flat_master,
    flat_first,
    flat_second,
    emb_master,
    emb_first,
    emb_second,
    norm_master,
    norm_first,
    norm_second,
    step_count,
):
    fsdp_count = lax.axis_size(FSDP)
    tp_count = lax.axis_size("tp")
    width = q_grad.shape[1]
    q_columns = q_grad.shape[2]
    entry_count = (
        2 * width * q_columns * tp_count
        + emb_grad.shape[0] * fsdp_count * width
        + norm_master.shape[0]
    )
    clip_limit = 0.5 * math.sqrt(entry_count)
    local_flat = jnp.concatenate([q_grad[0].reshape(-1), o_grad[0].reshape(-1)])
    piece_len = local_flat.shape[0] // fsdp_count
    core_count = lax.axis_size("c")
    halves = lax.all_to_all(
        local_flat.reshape(fsdp_count // core_count, core_count, piece_len), "c", 1, 1, tiled=True
    )
    partial = jnp.sum(halves.astype(jnp.float32), axis=1)
    pieces = lax.all_to_all(partial, ("z", "y"), 0, 0, tiled=True)
    grad_piece = jnp.sum(pieces, axis=0)
    emb_piece = lax.all_to_all(emb_grad, "tp", split_axis=0, concat_axis=1, tiled=True).astype(
        jnp.float32
    )
    emb_float = emb_grad.astype(jnp.float32)
    local_squares = jnp.sum(grad_piece * grad_piece) + jnp.sum(emb_float * emb_float)
    gains_local = norm_grad[0, 0]
    packed = jnp.concatenate([local_squares[None], gains_local])
    for axis in (("y", "c"), ("z", "tp")):
        count = lax.axis_size(axis)
        copies = jnp.broadcast_to(packed[None], (count,) + packed.shape)
        packed = jnp.sum(lax.all_to_all(copies, axis, 0, 0, tiled=True), axis=0)
    global_squares = packed[0]
    gain_sum = packed[1:]
    grad_norm = jnp.sqrt(global_squares + jnp.sum(gain_sum * gain_sum))
    clip_factor = jnp.minimum(jnp.float32(1.0), clip_limit / (grad_norm + 1e-06))
    step_value = step_count[0].astype(jnp.float32)
    first_fix = 1.0 - jnp.power(jnp.float32(BETA_ONE), step_value)
    second_fix = 1.0 - jnp.power(jnp.float32(BETA_TWO), step_value)
    flat_new, flat_one, flat_two = adam_update(
        flat_master[0],
        flat_first[0],
        flat_second[0],
        clip_factor * grad_piece,
        first_fix,
        second_fix,
        0.1,
    )
    emb_new, emb_one, emb_two = adam_update(
        emb_master, emb_first, emb_second, clip_factor * emb_piece, first_fix, second_fix, 0.1
    )
    norm_new, norm_one, norm_two = adam_update(
        norm_master, norm_first, norm_second, clip_factor * gain_sum, first_fix, second_fix, 0.0
    )
    gathered = lax.all_gather(flat_new.astype(jnp.bfloat16), ("y", "c"), axis=0, tiled=False)
    gathered = lax.all_gather(gathered, "z", axis=0, tiled=False).reshape(-1)
    q_weight = gathered[: width * q_columns].reshape(width, q_columns)
    o_weight = gathered[width * q_columns :].reshape(q_columns, width)
    block_rows = width // fsdp_count
    block_start = fsdp_index() * block_rows
    q_block = lax.dynamic_slice_in_dim(q_weight, block_start, block_rows, 0)
    o_block = lax.dynamic_slice_in_dim(o_weight, block_start, block_rows, 1)
    emb_rows = emb_new.astype(jnp.bfloat16)
    payload = jnp.concatenate([q_block.reshape(-1), o_block.reshape(-1), emb_rows.reshape(-1)])
    shared = lax.all_gather(payload, "tp", axis=0, tiled=False)
    q_len = block_rows * q_columns
    q_average = (
        shared[:, :q_len]
        .reshape(tp_count, block_rows, q_columns)
        .transpose(1, 0, 2)
        .reshape(block_rows, tp_count * q_columns)
    )
    o_average = shared[:, q_len : 2 * q_len].reshape(tp_count * q_columns, block_rows)
    emb_all = shared[:, 2 * q_len :].reshape(tp_count * emb_new.shape[0], width)
    emb_cols = width // tp_count
    emb_weight = lax.dynamic_slice_in_dim(emb_all, lax.axis_index("tp") * emb_cols, emb_cols, 1)
    return (
        flat_new[None, :],
        flat_one[None, :],
        flat_two[None, :],
        emb_new,
        emb_one,
        emb_two,
        norm_new,
        norm_one,
        norm_two,
        q_weight,
        o_weight,
        q_average,
        o_average,
        emb_weight,
    )


def solution(mesh):
    fsdp_count = mesh.shape["fsdp"]
    tp_count = mesh.shape["tp"]
    split = Mesh(
        mesh.devices.reshape(fsdp_count // (Y_SIZE * CORES), Y_SIZE, CORES, tp_count),
        ("z", "y", "c", "tp"),
    )
    both = FSDP + ("tp",)
    return jax.shard_map(
        body,
        mesh=split,
        in_specs=(
            P(FSDP, None, "tp"),
            P(FSDP, "tp", None),
            P(FSDP, "tp", None),
            P(FSDP, "tp"),
            P("tp", FSDP),
            P("tp", FSDP),
            P("tp", FSDP),
            P(both, None),
            P(both, None),
            P(both, None),
            P(),
            P(),
            P(),
            P(),
        ),
        out_specs=(
            P("tp", FSDP),
            P("tp", FSDP),
            P("tp", FSDP),
            P(both, None),
            P(both, None),
            P(both, None),
            P(),
            P(),
            P(),
            P(None, "tp"),
            P("tp", None),
            P(FSDP, None),
            P(None, FSDP),
            P(FSDP, "tp"),
        ),
        check_vma=False,
    )
```

```python
import math

import jax
import jax.numpy as jnp
from jax import lax
from jax.sharding import Mesh
from jax.sharding import PartitionSpec as P

BETA_ONE = 0.9
BETA_TWO = 0.95
EPSILON = 1e-08
LEARN_RATE = 0.0053

FSDP = ("z", "y", "c")
CORES = 2
Y_SIZE = 8


def adam_update(weights_in, first_in, second_in, gradient, first_fix, second_fix, decay_rate):
    first_out = BETA_ONE * first_in + (1.0 - BETA_ONE) * gradient
    second_out = BETA_TWO * second_in + (1.0 - BETA_TWO) * gradient * gradient
    update = first_out / first_fix / (jnp.sqrt(second_out / second_fix) + EPSILON)
    weights_out = weights_in - LEARN_RATE * (update + decay_rate * weights_in)
    return (weights_out, first_out, second_out)


def fsdp_index():
    return (
        lax.axis_index("z") * (Y_SIZE * CORES)
        + lax.axis_index("y") * CORES
        + lax.axis_index("c")
    )


def body(
    q_grad,
    o_grad,
    norm_grad,
    emb_grad,
    flat_master,
    flat_first,
    flat_second,
    emb_master,
    emb_first,
    emb_second,
    norm_master,
    norm_first,
    norm_second,
    step_count,
):
    fsdp_count = lax.axis_size(FSDP)
    tp_count = lax.axis_size("tp")
    width = q_grad.shape[1]
    q_columns = q_grad.shape[2]
    entry_count = (
        2 * width * q_columns * tp_count
        + emb_grad.shape[0] * fsdp_count * width
        + norm_master.shape[0]
    )
    clip_limit = 0.5 * math.sqrt(entry_count)
    local_flat = jnp.concatenate([q_grad[0].reshape(-1), o_grad[0].reshape(-1)])
    piece_len = local_flat.shape[0] // fsdp_count
    core_count = lax.axis_size("c")
    halves = lax.all_to_all(
        local_flat.reshape(fsdp_count // core_count, core_count, piece_len), "c", 1, 1, tiled=True
    )
    partial = jnp.sum(halves.astype(jnp.float32), axis=1)
    pieces = lax.all_to_all(partial, ("z", "y"), 0, 0, tiled=True)
    grad_piece = jnp.sum(pieces, axis=0)
    emb_float = emb_grad.astype(jnp.float32)
    local_squares = jnp.sum(grad_piece * grad_piece) + jnp.sum(emb_float * emb_float)
    gains_local = norm_grad[0, 0]
    packed = jnp.concatenate([local_squares[None], gains_local])
    def spread(values, axis):
        count = lax.axis_size(axis)
        copies = jnp.broadcast_to(values[None], (count,) + values.shape)
        return jnp.sum(lax.all_to_all(copies, axis, 0, 0, tiled=True), axis=0)

    packed = spread(packed, ("y", "c"))
    emb_blocks = emb_float.reshape(tp_count, -1)
    with_emb = jnp.concatenate(
        [jnp.broadcast_to(packed[None], (tp_count,) + packed.shape), emb_blocks], axis=1
    )
    received = lax.all_to_all(with_emb, "tp", 0, 0, tiled=True)
    packed = jnp.sum(received[:, : packed.shape[0]], axis=0)
    emb_rows_count = emb_grad.shape[0] // tp_count
    emb_piece = (
        received[:, packed.shape[0] :]
        .reshape(tp_count, emb_rows_count, emb_grad.shape[1])
        .transpose(1, 0, 2)
        .reshape(emb_rows_count, tp_count * emb_grad.shape[1])
    )
    packed = spread(packed, "z")
    global_squares = packed[0]
    gain_sum = packed[1:]
    grad_norm = jnp.sqrt(global_squares + jnp.sum(gain_sum * gain_sum))
    clip_factor = jnp.minimum(jnp.float32(1.0), clip_limit / (grad_norm + 1e-06))
    step_value = step_count[0].astype(jnp.float32)
    first_fix = 1.0 - jnp.power(jnp.float32(BETA_ONE), step_value)
    second_fix = 1.0 - jnp.power(jnp.float32(BETA_TWO), step_value)
    flat_new, flat_one, flat_two = adam_update(
        flat_master[0],
        flat_first[0],
        flat_second[0],
        clip_factor * grad_piece,
        first_fix,
        second_fix,
        0.1,
    )
    emb_new, emb_one, emb_two = adam_update(
        emb_master, emb_first, emb_second, clip_factor * emb_piece, first_fix, second_fix, 0.1
    )
    norm_new, norm_one, norm_two = adam_update(
        norm_master, norm_first, norm_second, clip_factor * gain_sum, first_fix, second_fix, 0.0
    )
    gathered = lax.all_gather(flat_new.astype(jnp.bfloat16), ("y", "c"), axis=0, tiled=False)
    gathered = lax.all_gather(gathered, "z", axis=0, tiled=False).reshape(-1)
    q_weight = gathered[: width * q_columns].reshape(width, q_columns)
    o_weight = gathered[width * q_columns :].reshape(q_columns, width)
    block_rows = width // fsdp_count
    block_start = fsdp_index() * block_rows
    q_block = lax.dynamic_slice_in_dim(q_weight, block_start, block_rows, 0)
    o_block = lax.dynamic_slice_in_dim(o_weight, block_start, block_rows, 1)
    emb_rows = emb_new.astype(jnp.bfloat16)
    payload = jnp.concatenate([q_block.reshape(-1), o_block.reshape(-1), emb_rows.reshape(-1)])
    shared = lax.all_gather(payload, "tp", axis=0, tiled=False)
    q_len = block_rows * q_columns
    q_average = (
        shared[:, :q_len]
        .reshape(tp_count, block_rows, q_columns)
        .transpose(1, 0, 2)
        .reshape(block_rows, tp_count * q_columns)
    )
    o_average = shared[:, q_len : 2 * q_len].reshape(tp_count * q_columns, block_rows)
    emb_all = shared[:, 2 * q_len :].reshape(tp_count * emb_new.shape[0], width)
    emb_cols = width // tp_count
    emb_weight = lax.dynamic_slice_in_dim(emb_all, lax.axis_index("tp") * emb_cols, emb_cols, 1)
    return (
        flat_new[None, :],
        flat_one[None, :],
        flat_two[None, :],
        emb_new,
        emb_one,
        emb_two,
        norm_new,
        norm_one,
        norm_two,
        q_weight,
        o_weight,
        q_average,
        o_average,
        emb_weight,
    )


def solution(mesh):
    fsdp_count = mesh.shape["fsdp"]
    tp_count = mesh.shape["tp"]
    split = Mesh(
        mesh.devices.reshape(fsdp_count // (Y_SIZE * CORES), Y_SIZE, CORES, tp_count),
        ("z", "y", "c", "tp"),
    )
    both = FSDP + ("tp",)
    return jax.shard_map(
        body,
        mesh=split,
        in_specs=(
            P(FSDP, None, "tp"),
            P(FSDP, "tp", None),
            P(FSDP, "tp", None),
            P(FSDP, "tp"),
            P("tp", FSDP),
            P("tp", FSDP),
            P("tp", FSDP),
            P(both, None),
            P(both, None),
            P(both, None),
            P(),
            P(),
            P(),
            P(),
        ),
        out_specs=(
            P("tp", FSDP),
            P("tp", FSDP),
            P("tp", FSDP),
            P(both, None),
            P(both, None),
            P(both, None),
            P(),
            P(),
            P(),
            P(None, "tp"),
            P("tp", None),
            P(FSDP, None),
            P(None, FSDP),
            P(FSDP, "tp"),
        ),
        check_vma=False,
    )
```

```python
import math

import jax
import jax.numpy as jnp
from jax import lax
from jax.sharding import Mesh
from jax.sharding import PartitionSpec as P

BETA_ONE = 0.9
BETA_TWO = 0.95
EPSILON = 1e-08
LEARN_RATE = 0.0053

FSDP = ("z", "y", "c")
CORES = 2
Y_SIZE = 8


def adam_update(weights_in, first_in, second_in, gradient, first_fix, second_fix, decay_rate):
    first_out = BETA_ONE * first_in + (1.0 - BETA_ONE) * gradient
    second_out = BETA_TWO * second_in + (1.0 - BETA_TWO) * gradient * gradient
    update = first_out / first_fix / (jnp.sqrt(second_out / second_fix) + EPSILON)
    weights_out = weights_in - LEARN_RATE * (update + decay_rate * weights_in)
    return (weights_out, first_out, second_out)


def fsdp_index():
    return (
        lax.axis_index("z") * (Y_SIZE * CORES)
        + lax.axis_index("y") * CORES
        + lax.axis_index("c")
    )


def body(
    q_grad,
    o_grad,
    norm_grad,
    emb_grad,
    flat_master,
    flat_first,
    flat_second,
    emb_master,
    emb_first,
    emb_second,
    norm_master,
    norm_first,
    norm_second,
    step_count,
):
    fsdp_count = lax.axis_size(FSDP)
    tp_count = lax.axis_size("tp")
    width = q_grad.shape[1]
    q_columns = q_grad.shape[2]
    entry_count = (
        2 * width * q_columns * tp_count
        + emb_grad.shape[0] * fsdp_count * width
        + norm_master.shape[0]
    )
    clip_limit = 0.5 * math.sqrt(entry_count)
    local_flat = jnp.concatenate([q_grad[0].reshape(-1), o_grad[0].reshape(-1)])
    piece_len = local_flat.shape[0] // fsdp_count
    core_count = lax.axis_size("c")
    halves = lax.all_to_all(
        local_flat.reshape(fsdp_count // core_count, core_count, piece_len), "c", 1, 1, tiled=True
    )
    partial = jnp.sum(halves.astype(jnp.float32), axis=1)
    pieces = lax.all_to_all(partial, ("z", "y"), 0, 0, tiled=True)
    grad_piece = jnp.sum(pieces, axis=0)
    tp_index = lax.axis_index("tp")
    emb_chunks = emb_grad.reshape(tp_count, emb_grad.shape[0] // tp_count, emb_grad.shape[1])
    by_shift = [emb_chunks[tp_index]]
    for shift in range(1, tp_count):
        outgoing = emb_chunks[(tp_index + shift) % tp_count]
        pairs = [(i, (i + shift) % tp_count) for i in range(tp_count)]
        by_shift.append(lax.ppermute(outgoing, "tp", pairs))
    by_shift = jnp.stack(by_shift)
    by_source = by_shift[(tp_index - jnp.arange(tp_count)) % tp_count]
    emb_piece = (
        by_source.transpose(1, 0, 2)
        .reshape(emb_chunks.shape[1], tp_count * emb_grad.shape[1])
        .astype(jnp.float32)
    )
    emb_float = emb_grad.astype(jnp.float32)
    local_squares = jnp.sum(grad_piece * grad_piece) + jnp.sum(emb_float * emb_float)
    gains_local = norm_grad[0, 0]
    packed = jnp.concatenate([local_squares[None], gains_local])
    for axis in (("y", "c"), ("z", "tp")):
        count = lax.axis_size(axis)
        copies = jnp.broadcast_to(packed[None], (count,) + packed.shape)
        packed = jnp.sum(lax.all_to_all(copies, axis, 0, 0, tiled=True), axis=0)
    global_squares = packed[0]
    gain_sum = packed[1:]
    grad_norm = jnp.sqrt(global_squares + jnp.sum(gain_sum * gain_sum))
    clip_factor = jnp.minimum(jnp.float32(1.0), clip_limit / (grad_norm + 1e-06))
    step_value = step_count[0].astype(jnp.float32)
    first_fix = 1.0 - jnp.power(jnp.float32(BETA_ONE), step_value)
    second_fix = 1.0 - jnp.power(jnp.float32(BETA_TWO), step_value)
    flat_new, flat_one, flat_two = adam_update(
        flat_master[0],
        flat_first[0],
        flat_second[0],
        clip_factor * grad_piece,
        first_fix,
        second_fix,
        0.1,
    )
    emb_new, emb_one, emb_two = adam_update(
        emb_master, emb_first, emb_second, clip_factor * emb_piece, first_fix, second_fix, 0.1
    )
    norm_new, norm_one, norm_two = adam_update(
        norm_master, norm_first, norm_second, clip_factor * gain_sum, first_fix, second_fix, 0.0
    )
    gathered = lax.all_gather(flat_new.astype(jnp.bfloat16), ("y", "c"), axis=0, tiled=False)
    gathered = lax.all_gather(gathered, "z", axis=0, tiled=False).reshape(-1)
    q_weight = gathered[: width * q_columns].reshape(width, q_columns)
    o_weight = gathered[width * q_columns :].reshape(q_columns, width)
    block_rows = width // fsdp_count
    block_start = fsdp_index() * block_rows
    q_block = lax.dynamic_slice_in_dim(q_weight, block_start, block_rows, 0)
    o_block = lax.dynamic_slice_in_dim(o_weight, block_start, block_rows, 1)
    emb_rows = emb_new.astype(jnp.bfloat16)
    payload = jnp.concatenate([q_block.reshape(-1), o_block.reshape(-1), emb_rows.reshape(-1)])
    shared = lax.all_to_all(
        jnp.broadcast_to(payload[None], (tp_count,) + payload.shape), "tp", 0, 0, tiled=True
    )
    q_len = block_rows * q_columns
    q_average = (
        shared[:, :q_len]
        .reshape(tp_count, block_rows, q_columns)
        .transpose(1, 0, 2)
        .reshape(block_rows, tp_count * q_columns)
    )
    o_average = shared[:, q_len : 2 * q_len].reshape(tp_count * q_columns, block_rows)
    emb_all = shared[:, 2 * q_len :].reshape(tp_count * emb_new.shape[0], width)
    emb_cols = width // tp_count
    emb_weight = lax.dynamic_slice_in_dim(emb_all, tp_index * emb_cols, emb_cols, 1)
    return (
        flat_new[None, :],
        flat_one[None, :],
        flat_two[None, :],
        emb_new,
        emb_one,
        emb_two,
        norm_new,
        norm_one,
        norm_two,
        q_weight,
        o_weight,
        q_average,
        o_average,
        emb_weight,
    )


def solution(mesh):
    fsdp_count = mesh.shape["fsdp"]
    tp_count = mesh.shape["tp"]
    split = Mesh(
        mesh.devices.reshape(fsdp_count // (Y_SIZE * CORES), Y_SIZE, CORES, tp_count),
        ("z", "y", "c", "tp"),
    )
    both = FSDP + ("tp",)
    return jax.shard_map(
        body,
        mesh=split,
        in_specs=(
            P(FSDP, None, "tp"),
            P(FSDP, "tp", None),
            P(FSDP, "tp", None),
            P(FSDP, "tp"),
            P("tp", FSDP),
            P("tp", FSDP),
            P("tp", FSDP),
            P(both, None),
            P(both, None),
            P(both, None),
            P(),
            P(),
            P(),
            P(),
        ),
        out_specs=(
            P("tp", FSDP),
            P("tp", FSDP),
            P("tp", FSDP),
            P(both, None),
            P(both, None),
            P(both, None),
            P(),
            P(),
            P(),
            P(None, "tp"),
            P("tp", None),
            P(FSDP, None),
            P(None, FSDP),
            P(FSDP, "tp"),
        ),
        check_vma=False,
    )
```

```python
import math

import jax
import jax.numpy as jnp
from jax import lax
from jax.sharding import Mesh
from jax.sharding import PartitionSpec as P

BETA_ONE = 0.9
BETA_TWO = 0.95
EPSILON = 1e-08
LEARN_RATE = 0.0053

FSDP = ("z", "y", "c")
CORES = 2
Y_SIZE = 8


def adam_update(weights_in, first_in, second_in, gradient, first_fix, second_fix, decay_rate):
    first_out = BETA_ONE * first_in + (1.0 - BETA_ONE) * gradient
    second_out = BETA_TWO * second_in + (1.0 - BETA_TWO) * gradient * gradient
    update = first_out / first_fix / (jnp.sqrt(second_out / second_fix) + EPSILON)
    weights_out = weights_in - LEARN_RATE * (update + decay_rate * weights_in)
    return (weights_out, first_out, second_out)


def fsdp_index():
    return (
        lax.axis_index("z") * (Y_SIZE * CORES)
        + lax.axis_index("y") * CORES
        + lax.axis_index("c")
    )


def body(
    q_grad,
    o_grad,
    norm_grad,
    emb_grad,
    flat_master,
    flat_first,
    flat_second,
    emb_master,
    emb_first,
    emb_second,
    norm_master,
    norm_first,
    norm_second,
    step_count,
):
    fsdp_count = lax.axis_size(FSDP)
    tp_count = lax.axis_size("tp")
    width = q_grad.shape[1]
    q_columns = q_grad.shape[2]
    entry_count = (
        2 * width * q_columns * tp_count
        + emb_grad.shape[0] * fsdp_count * width
        + norm_master.shape[0]
    )
    clip_limit = 0.5 * math.sqrt(entry_count)
    local_flat = jnp.concatenate([q_grad[0].reshape(-1), o_grad[0].reshape(-1)])
    piece_len = local_flat.shape[0] // fsdp_count
    core_count = lax.axis_size("c")
    halves = lax.all_to_all(
        local_flat.reshape(fsdp_count // core_count, core_count, piece_len), "c", 1, 1, tiled=True
    )
    partial = jnp.sum(halves.astype(jnp.float32), axis=1)
    pieces = lax.all_to_all(partial, ("z", "y"), 0, 0, tiled=True)
    grad_piece = jnp.sum(pieces, axis=0)
    emb_blocks = lax.all_gather(emb_grad, "tp", axis=0, tiled=False)
    emb_rows_count = emb_grad.shape[0] // tp_count
    emb_mine = lax.dynamic_slice_in_dim(
        emb_blocks, lax.axis_index("tp") * emb_rows_count, emb_rows_count, 1
    )
    emb_piece = (
        emb_mine.transpose(1, 0, 2)
        .reshape(emb_rows_count, tp_count * emb_grad.shape[1])
        .astype(jnp.float32)
    )
    emb_float = emb_grad.astype(jnp.float32)
    local_squares = jnp.sum(grad_piece * grad_piece) + jnp.sum(emb_float * emb_float)
    gains_local = norm_grad[0, 0]
    packed = jnp.concatenate([local_squares[None], gains_local])
    for axis in (("y", "c"), ("z", "tp")):
        count = lax.axis_size(axis)
        copies = jnp.broadcast_to(packed[None], (count,) + packed.shape)
        packed = jnp.sum(lax.all_to_all(copies, axis, 0, 0, tiled=True), axis=0)
    global_squares = packed[0]
    gain_sum = packed[1:]
    grad_norm = jnp.sqrt(global_squares + jnp.sum(gain_sum * gain_sum))
    clip_factor = jnp.minimum(jnp.float32(1.0), clip_limit / (grad_norm + 1e-06))
    step_value = step_count[0].astype(jnp.float32)
    first_fix = 1.0 - jnp.power(jnp.float32(BETA_ONE), step_value)
    second_fix = 1.0 - jnp.power(jnp.float32(BETA_TWO), step_value)
    flat_new, flat_one, flat_two = adam_update(
        flat_master[0],
        flat_first[0],
        flat_second[0],
        clip_factor * grad_piece,
        first_fix,
        second_fix,
        0.1,
    )
    emb_new, emb_one, emb_two = adam_update(
        emb_master, emb_first, emb_second, clip_factor * emb_piece, first_fix, second_fix, 0.1
    )
    norm_new, norm_one, norm_two = adam_update(
        norm_master, norm_first, norm_second, clip_factor * gain_sum, first_fix, second_fix, 0.0
    )
    gathered = lax.all_gather(flat_new.astype(jnp.bfloat16), ("y", "c"), axis=0, tiled=False)
    gathered = lax.all_gather(gathered, "z", axis=0, tiled=False).reshape(-1)
    q_weight = gathered[: width * q_columns].reshape(width, q_columns)
    o_weight = gathered[width * q_columns :].reshape(q_columns, width)
    block_rows = width // fsdp_count
    block_start = fsdp_index() * block_rows
    q_block = lax.dynamic_slice_in_dim(q_weight, block_start, block_rows, 0)
    o_block = lax.dynamic_slice_in_dim(o_weight, block_start, block_rows, 1)
    emb_rows = emb_new.astype(jnp.bfloat16)
    payload = jnp.concatenate([q_block.reshape(-1), o_block.reshape(-1), emb_rows.reshape(-1)])
    shared = lax.all_gather(payload, "tp", axis=0, tiled=False)
    q_len = block_rows * q_columns
    q_average = (
        shared[:, :q_len]
        .reshape(tp_count, block_rows, q_columns)
        .transpose(1, 0, 2)
        .reshape(block_rows, tp_count * q_columns)
    )
    o_average = shared[:, q_len : 2 * q_len].reshape(tp_count * q_columns, block_rows)
    emb_all = shared[:, 2 * q_len :].reshape(tp_count * emb_new.shape[0], width)
    emb_cols = width // tp_count
    emb_weight = lax.dynamic_slice_in_dim(emb_all, lax.axis_index("tp") * emb_cols, emb_cols, 1)
    return (
        flat_new[None, :],
        flat_one[None, :],
        flat_two[None, :],
        emb_new,
        emb_one,
        emb_two,
        norm_new,
        norm_one,
        norm_two,
        q_weight,
        o_weight,
        q_average,
        o_average,
        emb_weight,
    )


def solution(mesh):
    fsdp_count = mesh.shape["fsdp"]
    tp_count = mesh.shape["tp"]
    split = Mesh(
        mesh.devices.reshape(fsdp_count // (Y_SIZE * CORES), Y_SIZE, CORES, tp_count),
        ("z", "y", "c", "tp"),
    )
    both = FSDP + ("tp",)
    return jax.shard_map(
        body,
        mesh=split,
        in_specs=(
            P(FSDP, None, "tp"),
            P(FSDP, "tp", None),
            P(FSDP, "tp", None),
            P(FSDP, "tp"),
            P("tp", FSDP),
            P("tp", FSDP),
            P("tp", FSDP),
            P(both, None),
            P(both, None),
            P(both, None),
            P(),
            P(),
            P(),
            P(),
        ),
        out_specs=(
            P("tp", FSDP),
            P("tp", FSDP),
            P("tp", FSDP),
            P(both, None),
            P(both, None),
            P(both, None),
            P(),
            P(),
            P(),
            P(None, "tp"),
            P("tp", None),
            P(FSDP, None),
            P(None, FSDP),
            P(FSDP, "tp"),
        ),
        check_vma=False,
    )
```

```python
import math

import jax
import jax.numpy as jnp
from jax import lax
from jax.sharding import Mesh
from jax.sharding import PartitionSpec as P

BETA_ONE = 0.9
BETA_TWO = 0.95
EPSILON = 1e-08
LEARN_RATE = 0.0053

FSDP = ("z", "y", "c")
CORES = 2
Y_SIZE = 8


def adam_update(weights_in, first_in, second_in, gradient, first_fix, second_fix, decay_rate):
    first_out = BETA_ONE * first_in + (1.0 - BETA_ONE) * gradient
    second_out = BETA_TWO * second_in + (1.0 - BETA_TWO) * gradient * gradient
    update = first_out / first_fix / (jnp.sqrt(second_out / second_fix) + EPSILON)
    weights_out = weights_in - LEARN_RATE * (update + decay_rate * weights_in)
    return (weights_out, first_out, second_out)


def fsdp_index():
    return (
        lax.axis_index("z") * (Y_SIZE * CORES)
        + lax.axis_index("y") * CORES
        + lax.axis_index("c")
    )


def body(
    q_grad,
    o_grad,
    norm_grad,
    emb_grad,
    flat_master,
    flat_first,
    flat_second,
    emb_master,
    emb_first,
    emb_second,
    norm_master,
    norm_first,
    norm_second,
    step_count,
):
    fsdp_count = lax.axis_size(FSDP)
    tp_count = lax.axis_size("tp")
    width = q_grad.shape[1]
    q_columns = q_grad.shape[2]
    entry_count = (
        2 * width * q_columns * tp_count
        + emb_grad.shape[0] * fsdp_count * width
        + norm_master.shape[0]
    )
    clip_limit = 0.5 * math.sqrt(entry_count)
    local_flat = jnp.concatenate([q_grad[0].reshape(-1), o_grad[0].reshape(-1)])
    piece_len = local_flat.shape[0] // fsdp_count
    core_count = lax.axis_size("c")
    halves = lax.all_to_all(
        local_flat.reshape(fsdp_count // core_count, core_count, piece_len), "c", 1, 1, tiled=True
    )
    partial = jnp.sum(halves.astype(jnp.float32), axis=1)
    pieces = lax.all_to_all(partial, ("z", "y"), 0, 0, tiled=True)
    grad_piece = jnp.sum(pieces, axis=0)
    emb_blocks = lax.all_gather(emb_grad, "tp", axis=0, tiled=False)
    emb_rows_count = emb_grad.shape[0] // tp_count
    emb_mine = lax.dynamic_slice_in_dim(
        emb_blocks, lax.axis_index("tp") * emb_rows_count, emb_rows_count, 1
    )
    emb_piece = (
        emb_mine.transpose(1, 0, 2)
        .reshape(emb_rows_count, tp_count * emb_grad.shape[1])
        .astype(jnp.float32)
    )
    local_squares = jnp.sum(grad_piece * grad_piece) + jnp.sum(emb_piece * emb_piece)
    gains_local = norm_grad[0, 0]
    packed = jnp.concatenate([local_squares[None], gains_local])
    for axis in (("y", "c"), ("z", "tp")):
        count = lax.axis_size(axis)
        copies = jnp.broadcast_to(packed[None], (count,) + packed.shape)
        packed = jnp.sum(lax.all_to_all(copies, axis, 0, 0, tiled=True), axis=0)
    global_squares = packed[0]
    gain_sum = packed[1:]
    grad_norm = jnp.sqrt(global_squares + jnp.sum(gain_sum * gain_sum))
    clip_factor = jnp.minimum(jnp.float32(1.0), clip_limit / (grad_norm + 1e-06))
    step_value = step_count[0].astype(jnp.float32)
    first_fix = 1.0 - jnp.power(jnp.float32(BETA_ONE), step_value)
    second_fix = 1.0 - jnp.power(jnp.float32(BETA_TWO), step_value)
    flat_new, flat_one, flat_two = adam_update(
        flat_master[0],
        flat_first[0],
        flat_second[0],
        clip_factor * grad_piece,
        first_fix,
        second_fix,
        0.1,
    )
    emb_new, emb_one, emb_two = adam_update(
        emb_master, emb_first, emb_second, clip_factor * emb_piece, first_fix, second_fix, 0.1
    )
    norm_new, norm_one, norm_two = adam_update(
        norm_master, norm_first, norm_second, clip_factor * gain_sum, first_fix, second_fix, 0.0
    )
    gathered = lax.all_gather(flat_new.astype(jnp.bfloat16), ("y", "c"), axis=0, tiled=False)
    gathered = lax.all_gather(gathered, "z", axis=0, tiled=False).reshape(-1)
    q_weight = gathered[: width * q_columns].reshape(width, q_columns)
    o_weight = gathered[width * q_columns :].reshape(q_columns, width)
    block_rows = width // fsdp_count
    block_start = fsdp_index() * block_rows
    q_block = lax.dynamic_slice_in_dim(q_weight, block_start, block_rows, 0)
    o_block = lax.dynamic_slice_in_dim(o_weight, block_start, block_rows, 1)
    emb_rows = emb_new.astype(jnp.bfloat16)
    payload = jnp.concatenate([q_block.reshape(-1), o_block.reshape(-1), emb_rows.reshape(-1)])
    shared = lax.all_gather(payload, "tp", axis=0, tiled=False)
    q_len = block_rows * q_columns
    q_average = (
        shared[:, :q_len]
        .reshape(tp_count, block_rows, q_columns)
        .transpose(1, 0, 2)
        .reshape(block_rows, tp_count * q_columns)
    )
    o_average = shared[:, q_len : 2 * q_len].reshape(tp_count * q_columns, block_rows)
    emb_all = shared[:, 2 * q_len :].reshape(tp_count * emb_new.shape[0], width)
    emb_cols = width // tp_count
    emb_weight = lax.dynamic_slice_in_dim(emb_all, lax.axis_index("tp") * emb_cols, emb_cols, 1)
    return (
        flat_new[None, :],
        flat_one[None, :],
        flat_two[None, :],
        emb_new,
        emb_one,
        emb_two,
        norm_new,
        norm_one,
        norm_two,
        q_weight,
        o_weight,
        q_average,
        o_average,
        emb_weight,
    )


def solution(mesh):
    fsdp_count = mesh.shape["fsdp"]
    tp_count = mesh.shape["tp"]
    split = Mesh(
        mesh.devices.reshape(fsdp_count // (Y_SIZE * CORES), Y_SIZE, CORES, tp_count),
        ("z", "y", "c", "tp"),
    )
    both = FSDP + ("tp",)
    return jax.shard_map(
        body,
        mesh=split,
        in_specs=(
            P(FSDP, None, "tp"),
            P(FSDP, "tp", None),
            P(FSDP, "tp", None),
            P(FSDP, "tp"),
            P("tp", FSDP),
            P("tp", FSDP),
            P("tp", FSDP),
            P(both, None),
            P(both, None),
            P(both, None),
            P(),
            P(),
            P(),
            P(),
        ),
        out_specs=(
            P("tp", FSDP),
            P("tp", FSDP),
            P("tp", FSDP),
            P(both, None),
            P(both, None),
            P(both, None),
            P(),
            P(),
            P(),
            P(None, "tp"),
            P("tp", None),
            P(FSDP, None),
            P(None, FSDP),
            P(FSDP, "tp"),
        ),
        check_vma=False,
    )
```

```python
import math

import jax
import jax.numpy as jnp
from jax import lax
from jax.sharding import Mesh
from jax.sharding import PartitionSpec as P

BETA_ONE = 0.9
BETA_TWO = 0.95
EPSILON = 1e-08
LEARN_RATE = 0.0053

FSDP = ("z", "y", "c")
CORES = 2
Y_SIZE = 8


def adam_update(weights_in, first_in, second_in, gradient, first_fix, second_fix, decay_rate):
    first_out = BETA_ONE * first_in + (1.0 - BETA_ONE) * gradient
    second_out = BETA_TWO * second_in + (1.0 - BETA_TWO) * gradient * gradient
    update = first_out / first_fix / (jnp.sqrt(second_out / second_fix) + EPSILON)
    weights_out = weights_in - LEARN_RATE * (update + decay_rate * weights_in)
    return (weights_out, first_out, second_out)


def fsdp_index():
    return (
        lax.axis_index("z") * (Y_SIZE * CORES)
        + lax.axis_index("y") * CORES
        + lax.axis_index("c")
    )


def body(
    q_grad,
    o_grad,
    norm_grad,
    emb_grad,
    flat_master,
    flat_first,
    flat_second,
    emb_master,
    emb_first,
    emb_second,
    norm_master,
    norm_first,
    norm_second,
    step_count,
):
    fsdp_count = lax.axis_size(FSDP)
    tp_count = lax.axis_size("tp")
    width = q_grad.shape[1]
    q_columns = q_grad.shape[2]
    entry_count = (
        2 * width * q_columns * tp_count
        + emb_grad.shape[0] * fsdp_count * width
        + norm_master.shape[0]
    )
    clip_limit = 0.5 * math.sqrt(entry_count)
    local_flat = jnp.concatenate([q_grad[0].reshape(-1), o_grad[0].reshape(-1)])
    piece_len = local_flat.shape[0] // fsdp_count
    core_count = lax.axis_size("c")
    halves = lax.all_to_all(
        local_flat.reshape(fsdp_count // core_count, core_count, piece_len), "c", 1, 1, tiled=True
    )
    partial = jnp.sum(halves.astype(jnp.float32), axis=1)
    pieces = lax.all_to_all(partial, ("z", "y"), 0, 0, tiled=True)
    grad_piece = jnp.sum(pieces, axis=0)
    emb_blocks = lax.all_gather(emb_grad, "tp", axis=0, tiled=False)
    emb_rows_count = emb_grad.shape[0] // tp_count
    emb_mine = lax.dynamic_slice_in_dim(
        emb_blocks, lax.axis_index("tp") * emb_rows_count, emb_rows_count, 1
    )
    emb_piece = (
        emb_mine.transpose(1, 0, 2)
        .reshape(emb_rows_count, tp_count * emb_grad.shape[1])
        .astype(jnp.float32)
    )
    local_squares = jnp.sum(grad_piece * grad_piece) + jnp.sum(emb_piece * emb_piece)
    gains_local = norm_grad[0, 0]
    packed = jnp.concatenate([local_squares[None], gains_local])
    for axis in (("y", "c"), ("z", "tp")):
        count = lax.axis_size(axis)
        copies = jnp.broadcast_to(packed[None], (count,) + packed.shape)
        packed = jnp.sum(lax.all_to_all(copies, axis, 0, 0, tiled=True), axis=0)
    global_squares = packed[0]
    gain_sum = packed[1:]
    grad_norm = jnp.sqrt(global_squares + jnp.sum(gain_sum * gain_sum))
    clip_factor = jnp.minimum(jnp.float32(1.0), clip_limit / (grad_norm + 1e-06))
    step_value = step_count[0].astype(jnp.float32)
    first_fix = 1.0 - jnp.power(jnp.float32(BETA_ONE), step_value)
    second_fix = 1.0 - jnp.power(jnp.float32(BETA_TWO), step_value)
    flat_new, flat_one, flat_two = adam_update(
        flat_master[0],
        flat_first[0],
        flat_second[0],
        clip_factor * grad_piece,
        first_fix,
        second_fix,
        0.1,
    )
    emb_new, emb_one, emb_two = adam_update(
        emb_master, emb_first, emb_second, clip_factor * emb_piece, first_fix, second_fix, 0.1
    )
    norm_new, norm_one, norm_two = adam_update(
        norm_master, norm_first, norm_second, clip_factor * gain_sum, first_fix, second_fix, 0.0
    )
    gathered = lax.all_gather(flat_new.astype(jnp.bfloat16), ("y", "c"), axis=0, tiled=False)
    gathered = lax.all_gather(gathered, "z", axis=0, tiled=False).reshape(-1)
    q_weight = gathered[: width * q_columns].reshape(width, q_columns)
    o_weight = gathered[width * q_columns :].reshape(q_columns, width)
    block_rows = width // fsdp_count
    block_start = fsdp_index() * block_rows
    q_block = lax.dynamic_slice_in_dim(q_weight, block_start, block_rows, 0)
    o_block = lax.dynamic_slice_in_dim(o_weight, block_start, block_rows, 1)
    emb_rows = emb_new.astype(jnp.bfloat16)
    payload = jnp.concatenate([q_block.reshape(-1), o_block.reshape(-1), emb_rows.reshape(-1)])
    shared = lax.all_to_all(
        jnp.broadcast_to(payload[None], (tp_count,) + payload.shape), "tp", 0, 0, tiled=True
    )
    q_len = block_rows * q_columns
    q_average = (
        shared[:, :q_len]
        .reshape(tp_count, block_rows, q_columns)
        .transpose(1, 0, 2)
        .reshape(block_rows, tp_count * q_columns)
    )
    o_average = shared[:, q_len : 2 * q_len].reshape(tp_count * q_columns, block_rows)
    emb_all = shared[:, 2 * q_len :].reshape(tp_count * emb_new.shape[0], width)
    emb_cols = width // tp_count
    emb_weight = lax.dynamic_slice_in_dim(emb_all, lax.axis_index("tp") * emb_cols, emb_cols, 1)
    return (
        flat_new[None, :],
        flat_one[None, :],
        flat_two[None, :],
        emb_new,
        emb_one,
        emb_two,
        norm_new,
        norm_one,
        norm_two,
        q_weight,
        o_weight,
        q_average,
        o_average,
        emb_weight,
    )


def solution(mesh):
    fsdp_count = mesh.shape["fsdp"]
    tp_count = mesh.shape["tp"]
    split = Mesh(
        mesh.devices.reshape(fsdp_count // (Y_SIZE * CORES), Y_SIZE, CORES, tp_count),
        ("z", "y", "c", "tp"),
    )
    both = FSDP + ("tp",)
    return jax.shard_map(
        body,
        mesh=split,
        in_specs=(
            P(FSDP, None, "tp"),
            P(FSDP, "tp", None),
            P(FSDP, "tp", None),
            P(FSDP, "tp"),
            P("tp", FSDP),
            P("tp", FSDP),
            P("tp", FSDP),
            P(both, None),
            P(both, None),
            P(both, None),
            P(),
            P(),
            P(),
            P(),
        ),
        out_specs=(
            P("tp", FSDP),
            P("tp", FSDP),
            P("tp", FSDP),
            P(both, None),
            P(both, None),
            P(both, None),
            P(),
            P(),
            P(),
            P(None, "tp"),
            P("tp", None),
            P(FSDP, None),
            P(None, FSDP),
            P(FSDP, "tp"),
        ),
        check_vma=False,
    )
```

```python
import math

import jax
import jax.numpy as jnp
from jax import lax
from jax.sharding import Mesh
from jax.sharding import PartitionSpec as P

BETA_ONE = 0.9
BETA_TWO = 0.95
EPSILON = 1e-08
LEARN_RATE = 0.0053

FSDP = ("z", "y", "c")
CORES = 2
Y_SIZE = 8


def adam_update(weights_in, first_in, second_in, gradient, first_fix, second_fix, decay_rate):
    first_out = BETA_ONE * first_in + (1.0 - BETA_ONE) * gradient
    second_out = BETA_TWO * second_in + (1.0 - BETA_TWO) * gradient * gradient
    update = first_out / first_fix / (jnp.sqrt(second_out / second_fix) + EPSILON)
    weights_out = weights_in - LEARN_RATE * (update + decay_rate * weights_in)
    return (weights_out, first_out, second_out)


def fsdp_index():
    return (
        lax.axis_index("z") * (Y_SIZE * CORES)
        + lax.axis_index("y") * CORES
        + lax.axis_index("c")
    )


def body(
    q_grad,
    o_grad,
    norm_grad,
    emb_grad,
    flat_master,
    flat_first,
    flat_second,
    emb_master,
    emb_first,
    emb_second,
    norm_master,
    norm_first,
    norm_second,
    step_count,
):
    fsdp_count = lax.axis_size(FSDP)
    tp_count = lax.axis_size("tp")
    width = q_grad.shape[1]
    q_columns = q_grad.shape[2]
    entry_count = (
        2 * width * q_columns * tp_count
        + emb_grad.shape[0] * fsdp_count * width
        + norm_master.shape[0]
    )
    clip_limit = 0.5 * math.sqrt(entry_count)
    local_flat = jnp.concatenate([q_grad[0].reshape(-1), o_grad[0].reshape(-1)])
    piece_len = local_flat.shape[0] // fsdp_count
    core_count = lax.axis_size("c")
    halves = lax.all_to_all(
        local_flat.reshape(fsdp_count // core_count, core_count, piece_len), "c", 1, 1, tiled=True
    )
    partial = jnp.sum(halves.astype(jnp.float32), axis=1)
    pieces = lax.all_to_all(partial, ("z", "y"), 0, 0, tiled=True)
    grad_piece = jnp.sum(pieces, axis=0)
    emb_blocks = lax.all_gather(emb_grad, "tp", axis=0, tiled=False)
    emb_rows_count = emb_grad.shape[0] // tp_count
    emb_mine = lax.dynamic_slice_in_dim(
        emb_blocks, lax.axis_index("tp") * emb_rows_count, emb_rows_count, 1
    )
    emb_piece = (
        emb_mine.transpose(1, 0, 2)
        .reshape(emb_rows_count, tp_count * emb_grad.shape[1])
        .astype(jnp.float32)
    )
    local_squares = jnp.sum(grad_piece * grad_piece) + jnp.sum(emb_piece * emb_piece)
    gains_local = norm_grad[0, 0]
    packed = jnp.concatenate([local_squares[None], gains_local])
    for axis in (("z", "tp"), ("y", "c")):
        count = lax.axis_size(axis)
        copies = jnp.broadcast_to(packed[None], (count,) + packed.shape)
        packed = jnp.sum(lax.all_to_all(copies, axis, 0, 0, tiled=True), axis=0)
    global_squares = packed[0]
    gain_sum = packed[1:]
    grad_norm = jnp.sqrt(global_squares + jnp.sum(gain_sum * gain_sum))
    clip_factor = jnp.minimum(jnp.float32(1.0), clip_limit / (grad_norm + 1e-06))
    step_value = step_count[0].astype(jnp.float32)
    first_fix = 1.0 - jnp.power(jnp.float32(BETA_ONE), step_value)
    second_fix = 1.0 - jnp.power(jnp.float32(BETA_TWO), step_value)
    flat_new, flat_one, flat_two = adam_update(
        flat_master[0],
        flat_first[0],
        flat_second[0],
        clip_factor * grad_piece,
        first_fix,
        second_fix,
        0.1,
    )
    emb_new, emb_one, emb_two = adam_update(
        emb_master, emb_first, emb_second, clip_factor * emb_piece, first_fix, second_fix, 0.1
    )
    norm_new, norm_one, norm_two = adam_update(
        norm_master, norm_first, norm_second, clip_factor * gain_sum, first_fix, second_fix, 0.0
    )
    gathered = lax.all_gather(flat_new.astype(jnp.bfloat16), ("y", "c"), axis=0, tiled=False)
    gathered = lax.all_gather(gathered, "z", axis=0, tiled=False).reshape(-1)
    q_weight = gathered[: width * q_columns].reshape(width, q_columns)
    o_weight = gathered[width * q_columns :].reshape(q_columns, width)
    block_rows = width // fsdp_count
    block_start = fsdp_index() * block_rows
    q_block = lax.dynamic_slice_in_dim(q_weight, block_start, block_rows, 0)
    o_block = lax.dynamic_slice_in_dim(o_weight, block_start, block_rows, 1)
    emb_rows = emb_new.astype(jnp.bfloat16)
    payload = jnp.concatenate([q_block.reshape(-1), o_block.reshape(-1), emb_rows.reshape(-1)])
    shared = lax.all_gather(payload, "tp", axis=0, tiled=False)
    q_len = block_rows * q_columns
    q_average = (
        shared[:, :q_len]
        .reshape(tp_count, block_rows, q_columns)
        .transpose(1, 0, 2)
        .reshape(block_rows, tp_count * q_columns)
    )
    o_average = shared[:, q_len : 2 * q_len].reshape(tp_count * q_columns, block_rows)
    emb_all = shared[:, 2 * q_len :].reshape(tp_count * emb_new.shape[0], width)
    emb_cols = width // tp_count
    emb_weight = lax.dynamic_slice_in_dim(emb_all, lax.axis_index("tp") * emb_cols, emb_cols, 1)
    return (
        flat_new[None, :],
        flat_one[None, :],
        flat_two[None, :],
        emb_new,
        emb_one,
        emb_two,
        norm_new,
        norm_one,
        norm_two,
        q_weight,
        o_weight,
        q_average,
        o_average,
        emb_weight,
    )


def solution(mesh):
    fsdp_count = mesh.shape["fsdp"]
    tp_count = mesh.shape["tp"]
    split = Mesh(
        mesh.devices.reshape(fsdp_count // (Y_SIZE * CORES), Y_SIZE, CORES, tp_count),
        ("z", "y", "c", "tp"),
    )
    both = FSDP + ("tp",)
    return jax.shard_map(
        body,
        mesh=split,
        in_specs=(
            P(FSDP, None, "tp"),
            P(FSDP, "tp", None),
            P(FSDP, "tp", None),
            P(FSDP, "tp"),
            P("tp", FSDP),
            P("tp", FSDP),
            P("tp", FSDP),
            P(both, None),
            P(both, None),
            P(both, None),
            P(),
            P(),
            P(),
            P(),
        ),
        out_specs=(
            P("tp", FSDP),
            P("tp", FSDP),
            P("tp", FSDP),
            P(both, None),
            P(both, None),
            P(both, None),
            P(),
            P(),
            P(),
            P(None, "tp"),
            P("tp", None),
            P(FSDP, None),
            P(None, FSDP),
            P(FSDP, "tp"),
        ),
        check_vma=False,
    )
```

```python
import math

import jax
import jax.numpy as jnp
from jax import lax
from jax.sharding import Mesh
from jax.sharding import PartitionSpec as P

BETA_ONE = 0.9
BETA_TWO = 0.95
EPSILON = 1e-08
LEARN_RATE = 0.0053

FSDP = ("z", "y", "c")
CORES = 2
Y_SIZE = 8


def adam_update(weights_in, first_in, second_in, gradient, first_fix, second_fix, decay_rate):
    first_out = BETA_ONE * first_in + (1.0 - BETA_ONE) * gradient
    second_out = BETA_TWO * second_in + (1.0 - BETA_TWO) * gradient * gradient
    update = first_out / first_fix / (jnp.sqrt(second_out / second_fix) + EPSILON)
    weights_out = weights_in - LEARN_RATE * (update + decay_rate * weights_in)
    return (weights_out, first_out, second_out)


def fsdp_index():
    return (
        lax.axis_index("z") * (Y_SIZE * CORES)
        + lax.axis_index("y") * CORES
        + lax.axis_index("c")
    )


def body(
    q_grad,
    o_grad,
    norm_grad,
    emb_grad,
    flat_master,
    flat_first,
    flat_second,
    emb_master,
    emb_first,
    emb_second,
    norm_master,
    norm_first,
    norm_second,
    step_count,
):
    fsdp_count = lax.axis_size(FSDP)
    tp_count = lax.axis_size("tp")
    width = q_grad.shape[1]
    q_columns = q_grad.shape[2]
    entry_count = (
        2 * width * q_columns * tp_count
        + emb_grad.shape[0] * fsdp_count * width
        + norm_master.shape[0]
    )
    clip_limit = 0.5 * math.sqrt(entry_count)
    local_flat = jnp.concatenate([q_grad[0].reshape(-1), o_grad[0].reshape(-1)])
    piece_len = local_flat.shape[0] // fsdp_count
    core_count = lax.axis_size("c")
    halves = lax.all_to_all(
        local_flat.reshape(fsdp_count // core_count, core_count, piece_len), "c", 1, 1, tiled=True
    )
    partial = jnp.sum(halves.astype(jnp.float32), axis=1)
    pieces = lax.all_to_all(partial, ("z", "y"), 0, 0, tiled=True)
    grad_piece = jnp.sum(pieces, axis=0)
    emb_blocks = lax.all_gather(emb_grad, "tp", axis=0, tiled=False)
    emb_rows_count = emb_grad.shape[0] // tp_count
    emb_mine = lax.dynamic_slice_in_dim(
        emb_blocks, lax.axis_index("tp") * emb_rows_count, emb_rows_count, 1
    )
    emb_piece = (
        emb_mine.transpose(1, 0, 2)
        .reshape(emb_rows_count, tp_count * emb_grad.shape[1])
        .astype(jnp.float32)
    )
    local_squares = jnp.sum(grad_piece * grad_piece) + jnp.sum(emb_piece * emb_piece)
    gains_local = norm_grad[0, 0]
    packed = jnp.concatenate([local_squares[None], gains_local])
    for axis in (("z", "tp"), ("y", "c")):
        count = lax.axis_size(axis)
        copies = jnp.broadcast_to(packed[None], (count,) + packed.shape)
        packed = jnp.sum(lax.all_to_all(copies, axis, 0, 0, tiled=True), axis=0)
    global_squares = packed[0]
    gain_sum = packed[1:]
    grad_norm = jnp.sqrt(global_squares + jnp.sum(gain_sum * gain_sum))
    clip_factor = jnp.minimum(jnp.float32(1.0), clip_limit / (grad_norm + 1e-06))
    step_value = step_count[0].astype(jnp.float32)
    first_fix = 1.0 - jnp.power(jnp.float32(BETA_ONE), step_value)
    second_fix = 1.0 - jnp.power(jnp.float32(BETA_TWO), step_value)
    flat_new, flat_one, flat_two = adam_update(
        flat_master[0],
        flat_first[0],
        flat_second[0],
        clip_factor * grad_piece,
        first_fix,
        second_fix,
        0.1,
    )
    emb_new, emb_one, emb_two = adam_update(
        emb_master, emb_first, emb_second, clip_factor * emb_piece, first_fix, second_fix, 0.1
    )
    norm_new, norm_one, norm_two = adam_update(
        norm_master, norm_first, norm_second, clip_factor * gain_sum, first_fix, second_fix, 0.0
    )
    gathered = lax.all_gather(flat_new.astype(jnp.bfloat16), ("y", "c"), axis=0, tiled=False)
    gathered = lax.all_gather(gathered, "z", axis=0, tiled=False).reshape(-1)
    q_weight = gathered[: width * q_columns].reshape(width, q_columns)
    o_weight = gathered[width * q_columns :].reshape(q_columns, width)
    block_rows = width // fsdp_count
    block_start = fsdp_index() * block_rows
    q_block = lax.dynamic_slice_in_dim(q_weight, block_start, block_rows, 0)
    o_block = lax.dynamic_slice_in_dim(o_weight, block_start, block_rows, 1)
    emb_rows = emb_new.astype(jnp.bfloat16)
    payload = jnp.concatenate([q_block.reshape(-1), o_block.T.reshape(-1), emb_rows.reshape(-1)])
    shared = lax.all_gather(payload, "tp", axis=0, tiled=False)
    q_len = block_rows * q_columns
    q_average = (
        shared[:, :q_len]
        .reshape(tp_count, block_rows, q_columns)
        .transpose(1, 0, 2)
        .reshape(block_rows, tp_count * q_columns)
    )
    o_average = (
        shared[:, q_len : 2 * q_len]
        .reshape(tp_count, block_rows, q_columns)
        .transpose(1, 0, 2)
        .reshape(block_rows, tp_count * q_columns)
        .T
    )
    emb_all = shared[:, 2 * q_len :].reshape(tp_count * emb_new.shape[0], width)
    emb_cols = width // tp_count
    emb_weight = lax.dynamic_slice_in_dim(emb_all, lax.axis_index("tp") * emb_cols, emb_cols, 1)
    return (
        flat_new[None, :],
        flat_one[None, :],
        flat_two[None, :],
        emb_new,
        emb_one,
        emb_two,
        norm_new,
        norm_one,
        norm_two,
        q_weight,
        o_weight,
        q_average,
        o_average,
        emb_weight,
    )


def solution(mesh):
    fsdp_count = mesh.shape["fsdp"]
    tp_count = mesh.shape["tp"]
    split = Mesh(
        mesh.devices.reshape(fsdp_count // (Y_SIZE * CORES), Y_SIZE, CORES, tp_count),
        ("z", "y", "c", "tp"),
    )
    both = FSDP + ("tp",)
    return jax.shard_map(
        body,
        mesh=split,
        in_specs=(
            P(FSDP, None, "tp"),
            P(FSDP, "tp", None),
            P(FSDP, "tp", None),
            P(FSDP, "tp"),
            P("tp", FSDP),
            P("tp", FSDP),
            P("tp", FSDP),
            P(both, None),
            P(both, None),
            P(both, None),
            P(),
            P(),
            P(),
            P(),
        ),
        out_specs=(
            P("tp", FSDP),
            P("tp", FSDP),
            P("tp", FSDP),
            P(both, None),
            P(both, None),
            P(both, None),
            P(),
            P(),
            P(),
            P(None, "tp"),
            P("tp", None),
            P(FSDP, None),
            P(None, FSDP),
            P(FSDP, "tp"),
        ),
        check_vma=False,
    )
```
